32 devices in a mesh: pool: 8 (over z, x), col: 4 (over y, core).
Axes of the slice: x: 2, y: 2, z: 4, core: 2. Of those that a mesh axis runs over, the one named last changes fastest.
Arguments:
- elements: float32 [8, 128, 2048], P('pool', None, 'col'), may hold values from -6 to 6
- index_map: int32 [8, 2048], P('pool', 'col'), may hold values from 0 to 2047, as said below
- band_energy: float32 [8], P('pool'), may hold values from 0.5 to 3
- eval_energy: float32 [2], replicated, may hold values from -1 to 1
- pole_strength: float32 [2048, 2048], P(None, 'col'), may hold values from -0.0078125 to 0.0078125
- pole_frequency: float32 [2048, 2048], P(None, 'col'), may hold values from 0.5 to 4
Outputs:
- sigma: float32 [2, 128, 128], replicated
The draws below stay inside these ranges and needn't reach their ends.
Inputs may be any that keep to these rules, and one draw needn't show every extreme that they name: For every band, the entries of index_map in columns c * 512 to (c + 1) * 512 - 1 are those same indices in some order, for every column group c.
All inputs are finite; a program needn't handle non-finite values.
Results may differ from the reference program's by a relative error of at most 0.0003.
Values sent between devices are 32-bit elements; how exact they have to be, the bound alone decides.
No kernel may reach another device: no remote copies, remote signals or barrier semaphores. Data moves between devices by JAX's collectives and lax.ppermute only.
A program may use at most 64 MiB of HBM per device.

```python
import math
import jax
import jax.numpy as jnp
from jax import lax

NS = 128
NG = 2048
NE = 2
NB = 8
NGC = 512


def draw_index_map(key, part):
    groups = NG // NGC
    scores = jax.random.randint(key, (NB, groups, NGC), 0, 1 << 20) * NGC
    scores = scores + lax.broadcasted_iota(jnp.int32, (NB, groups, NGC), 2)
    within = jnp.argsort(scores, axis=2).astype(jnp.int32)
    offsets = lax.broadcasted_iota(jnp.int32, (NB, groups, NGC), 1) * NGC
    return (within + offsets).reshape(NB, NG).astype(jnp.int32)


def block_levels(key, shape, shards, least, high):
    def one(dim, parts):
        heights = jax.random.uniform(jax.random.fold_in(jax.random.fold_in(key, 6), dim), (parts,), jnp.float32, least / len(shards), high / len(shards))
        return jnp.repeat(jnp.exp(heights), shape[dim] // parts).reshape((-1,) + (1,) * (len(shape) - dim - 1))

    gain = one(*shards[0])
    for cut in shards[1:]:
        gain = gain * one(*cut)
    return gain


def bell_draw(key, shape, width, bound, split=(), held_as=jnp.bfloat16):
    level = block_levels(key, shape, split, -0.22, 0.18) if split else 1.0
    drawn = jax.random.normal(key, shape, jnp.float32) * width * level
    return jnp.minimum(jnp.maximum(drawn, -bound), bound).astype(held_as)


def setup_inputs(seed: int = 0) -> dict:
    keys = jax.random.split(jax.random.key(seed), 7)
    elements = bell_draw(keys[0], (NB, NS, NG), 1.0, 6.0, ((0, 8), (2, 4)), jnp.float32)
    index_map = draw_index_map(jax.random.fold_in(keys[6], 71), 0)
    band_energy = jnp.clip(0.5 + 2.5 * jax.random.uniform(keys[2], (NB,), jnp.float32) ** block_levels(keys[2], (NB,), ((0, 8),), -0.2, 0.2), 0.5, 3.0)
    eval_energy = jnp.clip(jax.random.uniform(keys[3], (NE,), jnp.float32, -1.0, 1.0), -1.0, 1.0)
    pole_strength = bell_draw(keys[4], (NG, NG), (1.0 / NG), 0.0078125, ((1, 4),), jnp.float32)
    pole_frequency = jnp.clip(jnp.exp(math.log(4.0) - 2.0794415 * jax.random.uniform(keys[5], (NG, NG), jnp.float32) ** block_levels(keys[5], (NG, NG), ((1, 4),), -0.2, 0.2)), 0.5, 4.0)
    return dict(elements=elements, index_map=index_map, band_energy=band_energy, eval_energy=eval_energy, pole_strength=pole_strength, pole_frequency=pole_frequency)


broadening = 0.5


def reference(elements, index_map, band_energy, eval_energy, pole_strength, pole_frequency):
    highest = lax.Precision.HIGHEST
    pole_weight = pole_strength / (2.0 * pole_frequency)

    def accumulate(running, band_data):
        stored, band_order, band_level = band_data
        ordered = jnp.take(stored, band_order.astype(jnp.int32), axis=1)
        offset = eval_energy[:, None, None] - band_level - pole_frequency[None]
        pole_tiles = pole_weight[None] * offset / (offset * offset + broadening * broadening)
        partial_value = jnp.einsum("mg,egh->emh", ordered, pole_tiles, precision=highest)
        return running + jnp.einsum("emh,nh->emn", partial_value, ordered, precision=highest), None

    start_value = jnp.zeros((NE, NS, NS), jnp.float32)
    result, unused = lax.scan(accumulate, start_value, (elements, index_map, band_energy))
    return result
```

```python
import jax
import jax.numpy as jnp
from jax import lax
from jax.sharding import PartitionSpec as P

broadening = 0.5


def permute_band(band_rows, band_index_row):
    highest = lax.Precision.HIGHEST
    columns = band_rows.shape[-1]
    source = lax.broadcasted_iota(jnp.int32, (columns, columns), 0)
    selector = (band_index_row[None, :] == source).astype(jnp.float32)
    return jnp.dot(band_rows, selector, precision=highest, preferred_element_type=jnp.float32)


def is_power_of_two(n):
    return n > 0 and (n & (n - 1)) == 0


def exchange(value, axis, size, partner):
    return lax.ppermute(value, axis, [(i, partner(i)) for i in range(size)])


def butterfly_sum(value, axes, size):
    stage = 1
    while stage < size:
        value = value + exchange(value, axes, size, lambda i, s=stage: i ^ s)
        stage *= 2
    return value


def make_local(col_size, total_size):
    def local(elements, index_map, band_energy, eval_energy, pole_strength, pole_frequency):
        highest = lax.Precision.HIGHEST
        columns = elements.shape[2]
        energies = eval_energy.shape[0]
        column_group = lax.axis_index("col")
        local_index = index_map - column_group * columns
        ordered = permute_band(elements[0], local_index[0])

        if is_power_of_two(col_size):
            sources = [(0, column_group)] + [
                (m, column_group ^ m) for m in range(1, col_size)
            ]
            partner = lambda m: (lambda i: i ^ m)
        else:
            sources = [(0, column_group)] + [
                (m, (column_group + col_size - m) % col_size) for m in range(1, col_size)
            ]
            partner = lambda m: (lambda i: (i + m) % col_size)
        blocks = {0: ordered}
        for m, _ in sources[1:]:
            blocks[m] = exchange(ordered, "col", col_size, partner(m))

        pole_weight = pole_strength / (2.0 * pole_frequency)
        band_level = band_energy[0]
        sigmas = []
        for energy in range(energies):
            mixed = None
            for m, owner in sources:
                start = owner * columns
                weight_rows = lax.dynamic_slice_in_dim(pole_weight, start, columns, axis=0)
                frequency_rows = lax.dynamic_slice_in_dim(pole_frequency, start, columns, axis=0)
                offset = eval_energy[energy] - band_level - frequency_rows
                tile_now = weight_rows * offset / (offset * offset + broadening * broadening)
                part = jnp.dot(blocks[m], tile_now, precision=highest, preferred_element_type=jnp.float32)
                mixed = part if mixed is None else mixed + part
            sigmas.append(
                jnp.dot(mixed, ordered.T, precision=highest, preferred_element_type=jnp.float32)
            )
        local_sigma = jnp.stack(sigmas)
        if is_power_of_two(total_size):
            return butterfly_sum(local_sigma, ("pool", "col"), total_size)
        return lax.psum(local_sigma, ("pool", "col"))

    return local


def solution(mesh):
    placed = (
        P("pool", None, "col"),
        P("pool", "col"),
        P("pool"),
        P(),
        P(None, "col"),
        P(None, "col"),
    )
    col_size = mesh.shape["col"]
    total_size = mesh.shape["pool"] * col_size
    return jax.shard_map(
        make_local(col_size, total_size), mesh=mesh, in_specs=placed, out_specs=P(), check_vma=False
    )
```

```python
import jax
import jax.numpy as jnp
from jax import lax
from jax.sharding import PartitionSpec as P

broadening = 0.5


def permute_band(band_rows, band_index_row):
    highest = lax.Precision.HIGHEST
    columns = band_rows.shape[-1]
    source = lax.broadcasted_iota(jnp.int32, (columns, columns), 0)
    selector = (band_index_row[None, :] == source).astype(jnp.float32)
    return jnp.dot(band_rows, selector, precision=highest, preferred_element_type=jnp.float32)


def is_power_of_two(n):
    return n > 0 and (n & (n - 1)) == 0


def exchange(value, axis, size, partner):
    return lax.ppermute(value, axis, [(i, partner(i)) for i in range(size)])


def butterfly_sum(value, axes, size):
    stage = 1
    while stage < size:
        value = value + exchange(value, axes, size, lambda i, s=stage: i ^ s)
        stage *= 2
    return value


def make_local(col_size, total_size):
    def local(elements, index_map, band_energy, eval_energy, pole_strength, pole_frequency):
        highest = lax.Precision.HIGHEST
        columns = elements.shape[2]
        energies = eval_energy.shape[0]
        column_group = lax.axis_index("col")
        local_index = index_map - column_group * columns
        ordered = permute_band(elements[0], local_index[0])

        if is_power_of_two(col_size):
            sources = [(0, column_group)] + [
                (m, column_group ^ m) for m in range(1, col_size)
            ]
            partner = lambda m: (lambda i: i ^ m)
        else:
            sources = [(0, column_group)] + [
                (m, (column_group + col_size - m) % col_size) for m in range(1, col_size)
            ]
            partner = lambda m: (lambda i: (i + m) % col_size)
        blocks = {0: ordered}
        for m, _ in sources[1:]:
            blocks[m] = exchange(ordered, "col", col_size, partner(m))

        band_level = band_energy[0]
        sigmas = []
        for energy in range(energies):
            mixed = None
            for m, owner in sources:
                start = owner * columns
                strength_rows = lax.dynamic_slice_in_dim(pole_strength, start, columns, axis=0)
                frequency_rows = lax.dynamic_slice_in_dim(pole_frequency, start, columns, axis=0)
                offset = eval_energy[energy] - band_level - frequency_rows
                denominator = 2.0 * frequency_rows * (offset * offset + broadening * broadening)
                tile_now = strength_rows * offset / denominator
                part = jnp.dot(blocks[m], tile_now, precision=highest, preferred_element_type=jnp.float32)
                mixed = part if mixed is None else mixed + part
            sigma = jnp.dot(mixed, ordered.T, precision=highest, preferred_element_type=jnp.float32)
            if is_power_of_two(total_size):
                sigma = butterfly_sum(sigma, ("pool", "col"), total_size)
            else:
                sigma = lax.psum(sigma, ("pool", "col"))
            sigmas.append(sigma)
        return jnp.stack(sigmas)

    return local


def solution(mesh):
    placed = (
        P("pool", None, "col"),
        P("pool", "col"),
        P("pool"),
        P(),
        P(None, "col"),
        P(None, "col"),
    )
    col_size = mesh.shape["col"]
    total_size = mesh.shape["pool"] * col_size
    return jax.shard_map(
        make_local(col_size, total_size), mesh=mesh, in_specs=placed, out_specs=P(), check_vma=False
    )
```

```python
import jax
import jax.numpy as jnp
from jax import lax
from jax.sharding import PartitionSpec as P

broadening = 0.5


def permute_band(band_rows, band_index_row):
    highest = lax.Precision.HIGHEST
    columns = band_rows.shape[-1]
    source = lax.broadcasted_iota(jnp.int32, (columns, columns), 0)
    selector = (band_index_row[None, :] == source).astype(jnp.float32)
    return jnp.dot(band_rows, selector, precision=highest, preferred_element_type=jnp.float32)


def is_power_of_two(n):
    return n > 0 and (n & (n - 1)) == 0


def exchange(value, axis, size, partner):
    return lax.ppermute(value, axis, [(i, partner(i)) for i in range(size)])


def butterfly_sum(value, axes, size):
    stage = 1
    while stage < size:
        value = value + exchange(value, axes, size, lambda i, s=stage: i ^ s)
        stage *= 2
    return value


def make_local(col_size, total_size):
    def local(elements, index_map, band_energy, eval_energy, pole_strength, pole_frequency):
        high = lax.Precision.HIGH
        columns = elements.shape[2]
        energies = eval_energy.shape[0]
        column_group = lax.axis_index("col")
        local_index = index_map - column_group * columns
        ordered = permute_band(elements[0], local_index[0])

        if is_power_of_two(col_size):
            sources = [(0, column_group)] + [
                (m, column_group ^ m) for m in range(1, col_size)
            ]
            partner = lambda m: (lambda i: i ^ m)
        else:
            sources = [(0, column_group)] + [
                (m, (column_group + col_size - m) % col_size) for m in range(1, col_size)
            ]
            partner = lambda m: (lambda i: (i + m) % col_size)
        blocks = {0: ordered}
        for m, _ in sources[1:]:
            blocks[m] = exchange(ordered, "col", col_size, partner(m))

        band_level = band_energy[0]
        sigmas = []
        for energy in range(energies):
            mixed = None
            for m, owner in sources:
                start = owner * columns
                strength_rows = lax.dynamic_slice_in_dim(pole_strength, start, columns, axis=0)
                frequency_rows = lax.dynamic_slice_in_dim(pole_frequency, start, columns, axis=0)
                offset = eval_energy[energy] - band_level - frequency_rows
                denominator = 2.0 * frequency_rows * (offset * offset + broadening * broadening)
                tile_now = strength_rows * offset / denominator
                part = jnp.dot(blocks[m], tile_now, precision=high, preferred_element_type=jnp.float32)
                mixed = part if mixed is None else mixed + part
            sigma = jnp.dot(mixed, ordered.T, precision=high, preferred_element_type=jnp.float32)
            if is_power_of_two(total_size):
                sigma = butterfly_sum(sigma, ("pool", "col"), total_size)
            else:
                sigma = lax.psum(sigma, ("pool", "col"))
            sigmas.append(sigma)
        return jnp.stack(sigmas)

    return local


def solution(mesh):
    placed = (
        P("pool", None, "col"),
        P("pool", "col"),
        P("pool"),
        P(),
        P(None, "col"),
        P(None, "col"),
    )
    col_size = mesh.shape["col"]
    total_size = mesh.shape["pool"] * col_size
    return jax.shard_map(
        make_local(col_size, total_size), mesh=mesh, in_specs=placed, out_specs=P(), check_vma=False
    )
```

```python
import jax
import jax.numpy as jnp
from jax import lax
from jax.sharding import PartitionSpec as P

broadening = 0.5


def permute_band(band_rows, band_index_row):
    highest = lax.Precision.HIGHEST
    columns = band_rows.shape[-1]
    source = lax.broadcasted_iota(jnp.int32, (columns, columns), 0)
    selector = (band_index_row[None, :] == source).astype(jnp.float32)
    return jnp.dot(band_rows, selector, precision=highest, preferred_element_type=jnp.float32)


def is_power_of_two(n):
    return n > 0 and (n & (n - 1)) == 0


def exchange(value, axis, size, partner):
    return lax.ppermute(value, axis, [(i, partner(i)) for i in range(size)])


def butterfly_sum(value, axes, size):
    stage = 1
    while stage < size:
        value = value + exchange(value, axes, size, lambda i, s=stage: i ^ s)
        stage *= 2
    return value


def make_local(col_size, total_size):
    def local(elements, index_map, band_energy, eval_energy, pole_strength, pole_frequency):
        high = lax.Precision.HIGH
        columns = elements.shape[2]
        energies = eval_energy.shape[0]
        column_group = lax.axis_index("col")
        local_index = index_map - column_group * columns
        ordered = permute_band(elements[0], local_index[0])

        if is_power_of_two(col_size):
            held = [(0, ordered)]
            stage = col_size // 2
            while stage >= 1:
                stacked = jnp.stack([value for _, value in held])
                arrived = exchange(stacked, "col", col_size, lambda i, s=stage: i ^ s)
                held = held + [(mask ^ stage, arrived[k]) for k, (mask, _) in enumerate(held)]
                stage //= 2
            sources = [(column_group ^ mask, value) for mask, value in held]
        else:
            sources = [(column_group, ordered)] + [
                ((column_group + col_size - m) % col_size,
                 exchange(ordered, "col", col_size, lambda i, m=m: (i + m) % col_size))
                for m in range(1, col_size)
            ]

        band_level = band_energy[0]
        mixed = [None] * energies
        for owner, block in sources:
            start = owner * columns
            strength_rows = lax.dynamic_slice_in_dim(pole_strength, start, columns, axis=0)
            frequency_rows = lax.dynamic_slice_in_dim(pole_frequency, start, columns, axis=0)
            for energy in range(energies):
                offset = eval_energy[energy] - band_level - frequency_rows
                denominator = 2.0 * frequency_rows * (offset * offset + broadening * broadening)
                tile_now = strength_rows * offset / denominator
                part = jnp.dot(block, tile_now, precision=high, preferred_element_type=jnp.float32)
                mixed[energy] = part if mixed[energy] is None else mixed[energy] + part
        sigmas = []
        for energy in range(energies):
            sigma = jnp.dot(mixed[energy], ordered.T, precision=high, preferred_element_type=jnp.float32)
            if is_power_of_two(total_size):
                sigma = butterfly_sum(sigma, ("pool", "col"), total_size)
            else:
                sigma = lax.psum(sigma, ("pool", "col"))
            sigmas.append(sigma)
        return jnp.stack(sigmas)

    return local


def solution(mesh):
    placed = (
        P("pool", None, "col"),
        P("pool", "col"),
        P("pool"),
        P(),
        P(None, "col"),
        P(None, "col"),
    )
    col_size = mesh.shape["col"]
    total_size = mesh.shape["pool"] * col_size
    return jax.shard_map(
        make_local(col_size, total_size), mesh=mesh, in_specs=placed, out_specs=P(), check_vma=False
    )
```

```python
import jax
import jax.numpy as jnp
from jax import lax
from jax.sharding import PartitionSpec as P

broadening = 0.5


def permute_band(band_rows, band_index_row):
    highest = lax.Precision.HIGHEST
    columns = band_rows.shape[-1]
    source = lax.broadcasted_iota(jnp.int32, (columns, columns), 0)
    selector = (band_index_row[None, :] == source).astype(jnp.float32)
    return jnp.dot(band_rows, selector, precision=highest, preferred_element_type=jnp.float32)


def is_power_of_two(n):
    return n > 0 and (n & (n - 1)) == 0


def exchange(value, axis, size, partner):
    return lax.ppermute(value, axis, [(i, partner(i)) for i in range(size)])


def butterfly_sum(value, axes, size):
    stage = 1
    while stage < size:
        value = value + exchange(value, axes, size, lambda i, s=stage: i ^ s)
        stage *= 2
    return value


def make_local(col_size, total_size):
    def local(elements, index_map, band_energy, eval_energy, pole_strength, pole_frequency):
        high = lax.Precision.HIGH
        columns = elements.shape[2]
        energies = eval_energy.shape[0]
        column_group = lax.axis_index("col")
        local_index = index_map - column_group * columns
        ordered = permute_band(elements[0], local_index[0])

        band_level = band_energy[0]
        states = ordered.shape[0]
        halves = 2 if states % 16 == 0 else 1
        rows = states // halves
        results = []
        for half in range(halves):
            own_rows = ordered[half * rows:(half + 1) * rows]
            if is_power_of_two(col_size):
                held = [(0, own_rows)]
                stage = col_size // 2
                while stage >= 1:
                    stacked = jnp.stack([value for _, value in held])
                    arrived = exchange(stacked, "col", col_size, lambda i, s=stage: i ^ s)
                    held = held + [(mask ^ stage, arrived[k]) for k, (mask, _) in enumerate(held)]
                    stage //= 2
                sources = [(column_group ^ mask, value) for mask, value in held]
            else:
                sources = [(column_group, own_rows)] + [
                    ((column_group + col_size - m) % col_size,
                     exchange(own_rows, "col", col_size, lambda i, m=m: (i + m) % col_size))
                    for m in range(1, col_size)
                ]
            mixed = [None] * energies
            for owner, block in sources:
                start = owner * columns
                strength_rows = lax.dynamic_slice_in_dim(pole_strength, start, columns, axis=0)
                frequency_rows = lax.dynamic_slice_in_dim(pole_frequency, start, columns, axis=0)
                for energy in range(energies):
                    offset = eval_energy[energy] - band_level - frequency_rows
                    denominator = 2.0 * frequency_rows * (offset * offset + broadening * broadening)
                    tile_now = strength_rows * offset / denominator
                    part = jnp.dot(block, tile_now, precision=high, preferred_element_type=jnp.float32)
                    mixed[energy] = part if mixed[energy] is None else mixed[energy] + part
            sigma = jnp.stack([
                jnp.dot(mixed[energy], ordered.T, precision=high, preferred_element_type=jnp.float32)
                for energy in range(energies)
            ])
            if is_power_of_two(total_size):
                sigma = butterfly_sum(sigma, ("pool", "col"), total_size)
            else:
                sigma = lax.psum(sigma, ("pool", "col"))
            results.append(sigma)
        return jnp.concatenate(results, axis=1)

    return local


def solution(mesh):
    placed = (
        P("pool", None, "col"),
        P("pool", "col"),
        P("pool"),
        P(),
        P(None, "col"),
        P(None, "col"),
    )
    col_size = mesh.shape["col"]
    total_size = mesh.shape["pool"] * col_size
    return jax.shard_map(
        make_local(col_size, total_size), mesh=mesh, in_specs=placed, out_specs=P(), check_vma=False
    )
```
